128 devices in a mesh: occ: 8 (over z_lo, y), aux: 16 (over z_hi, x, core).
Axes of the slice: x: 4, y: 4, z: 4 (z_hi: 2, z_lo: 2; z = z_hi * 2 + z_lo), core: 2. Of those that a mesh axis runs over, the one named last changes fastest.
Arguments:
- factors: float32 [16384, 8, 768], P('aux', 'occ'), may hold values from -1.25 to 1.25
- eps_occ: float32 [8], replicated, may hold values from -2 to -0.5
- eps_vir: float32 [768], replicated, may hold values from 0.5 to 3
Outputs:
- density: float32 [16384, 8, 768], P('aux', 'occ')
The draws below stay inside these ranges and needn't reach their ends.
All inputs are finite; a program needn't handle non-finite values.
Results may differ from the reference program's by a relative error of at most 0.0003.
Values sent between devices are 32-bit elements; how exact they have to be, the bound alone decides.
No kernel may reach another device: no remote copies, remote signals or barrier semaphores. Data moves between devices by JAX's collectives and lax.ppermute only.
A program may use at most 128 MiB of HBM per device.

```python
import jax
import jax.numpy as jnp
from jax import lax

OCC_DEV = 1
NV = 768
NAUX = 16384
NOCC = 8
N_OCC = 8


def block_scale(stream_key, extent, shards, smallest, largest):
    loudness = 1.0
    for axis_at, shards_of in shards:
        heights = jax.random.uniform(jax.random.fold_in(jax.random.fold_in(stream_key, 6), axis_at), (shards_of,), jnp.float32, smallest / len(shards), largest / len(shards))
        loudness = loudness * jnp.repeat(jnp.exp(heights), extent[axis_at] // shards_of).reshape((-1,) + (1,) * (len(extent) - 1 - axis_at))
    return loudness


def centred(stream_key, dims, spread, most, shards=(), kind=jnp.bfloat16):
    factor_of = block_scale(stream_key, dims, shards, -0.22, 0.18) if shards else 1.0
    result = jax.random.normal(stream_key, dims, jnp.float32) * spread * factor_of
    return jnp.minimum(jnp.maximum(result, -most), most).astype(kind)


def setup_inputs(seed: int = 0) -> dict:
    seeds = jax.random.split(jax.random.key(seed), 4)
    factors = centred(seeds[0], (NAUX, NOCC, NV), (1.0 / (NAUX ** 0.25)), 1.25, ((0, 16), (1, 8)), jnp.float32)
    eps_occ = jnp.clip(jax.random.uniform(seeds[1], (NOCC,), jnp.float32, -2.0, -0.5), -2.0, -0.5)
    eps_vir = jnp.clip(jax.random.uniform(seeds[2], (NV,), jnp.float32, 0.5, 3.0), 0.5, 3.0)
    return dict(factors=factors, eps_occ=eps_occ, eps_vir=eps_vir)


def reference(factors, eps_occ, eps_vir):
    width = OCC_DEV * NV
    flat = factors.reshape(NAUX, N_OCC, width)
    energies = eps_occ.reshape(N_OCC, OCC_DEV)

    def pair_vals(group):
        occ_part = lax.dynamic_index_in_dim(energies, group, 0, keepdims=False)
        return (occ_part[:, None] - eps_vir[None, :]).reshape(width)

    def one_group(group):
        own = lax.dynamic_index_in_dim(flat, group, 1, keepdims=False)
        own_vals = pair_vals(group)
        total = jnp.zeros((NAUX, width), jnp.float32)
        for offset in (-1, 0, 1):
            partner = ((group + offset + N_OCC) % N_OCC).astype(jnp.int32)
            other = lax.dynamic_index_in_dim(flat, partner, 1, keepdims=False)
            other_vals = pair_vals(partner)
            integral = jnp.dot(own.T, other, precision=lax.Precision.HIGHEST, preferred_element_type=jnp.float32)
            amplitude = integral / (own_vals[:, None] + other_vals[None, :])
            total = total + jnp.dot(other, amplitude.T, precision=lax.Precision.HIGHEST, preferred_element_type=jnp.float32)
        return 1.3 * total

    groups = lax.map(one_group, jnp.arange(N_OCC, dtype=jnp.int32))
    return jnp.transpose(groups, (1, 0, 2)).reshape(NAUX, N_OCC * OCC_DEV, NV)
```

```python
import jax
import jax.numpy as jnp
import numpy as np
from jax import lax
from jax.sharding import PartitionSpec as P

PREC = lax.Precision.HIGHEST


def passed_along(value, axis, steps):
    count = lax.axis_size(axis)
    pairs = [(source, (source + steps) % count) for source in range(count)]
    return lax.ppermute(value, axis, pairs)


def pair_values(eps_occ, eps_vir, group, occ_dev):
    occ_part = lax.dynamic_slice_in_dim(eps_occ, group * occ_dev, occ_dev)
    return (occ_part[:, None] - eps_vir[None, :]).reshape(-1)


def aux_stages(count):
    assert count == 16
    stages = []
    core = [(i ^ 1, i & 1) for i in range(count)]
    stages.append(core)

    def x_of(i):
        return (i >> 1) & 3

    def with_x(i, x):
        return (i & ~6) | (x << 1)

    first, second = [], []
    for i in range(count):
        x = x_of(i)
        if i & 1 == 0:
            first.append((with_x(i, x ^ 1), (x & 1) ^ (x >> 1)))
            second.append((with_x(i, 3 - x), x >> 1))
        else:
            first.append((with_x(i, 3 - x), x >> 1))
            second.append((with_x(i, x ^ 1), x & 1))
    stages.append(first)
    stages.append(second)
    stages.append([(i ^ 8, (i >> 3) & 1) for i in range(count)])
    for s, stage in enumerate(stages):
        for i, (j, k) in enumerate(stage):
            assert stage[j][0] == i and stage[j][1] != k
            for t in range(s):
                assert stages[t][i][1] == stages[t][j][1]
    share = [0] * count
    for i in range(count):
        for stage in stages:
            share[i] = share[i] * 2 + stage[i][1]
    assert sorted(share) == list(range(count))
    return stages, share


def keep_bits(stages, share):
    table = np.array([[stage[i][1] for stage in stages] for i in range(len(share))], np.int32)
    idx = lax.axis_index("aux")
    bits = jnp.asarray(table)[idx]
    return [bits[s] for s in range(len(stages))], jnp.asarray(np.array(share, np.int32))[idx]


def reduce_scatter_rows(value, stages, bits):
    for stage, bit in zip(stages, bits):
        half = value.shape[0] // 2
        pairs = [(i, j) for i, (j, _) in enumerate(stage)]
        keep = lax.dynamic_slice_in_dim(value, bit * half, half, 0)
        send = lax.dynamic_slice_in_dim(value, (1 - bit) * half, half, 0)
        value = keep + lax.ppermute(send, "aux", pairs)
    return value


def all_gather_rows(value, stages, bits):
    for stage, bit in reversed(list(zip(stages, bits))):
        rows = value.shape[0]
        pairs = [(i, j) for i, (j, _) in enumerate(stage)]
        got = lax.ppermute(value, "aux", pairs)
        out = jnp.zeros((2 * rows,) + value.shape[1:], value.dtype)
        out = lax.dynamic_update_slice_in_dim(out, value, bit * rows, 0)
        value = lax.dynamic_update_slice_in_dim(out, got, (1 - bit) * rows, 0)
    return value


def body(factors, eps_occ, eps_vir):
    aux_dev, occ_dev, virt = factors.shape
    width = occ_dev * virt
    group = lax.axis_index("occ")
    groups = lax.axis_size("occ")
    aux_count = lax.axis_size("aux")
    stages, share = aux_stages(aux_count)
    bits, my_share = keep_bits(stages, share)
    rows = width // aux_count

    own = factors.reshape(aux_dev, width)
    below = passed_along(factors, "occ", 1).reshape(aux_dev, width)
    above = passed_along(factors, "occ", -1).reshape(aux_dev, width)

    own_vals = pair_values(eps_occ, eps_vir, group, occ_dev)
    up_vals = pair_values(eps_occ, eps_vir, (group + 1) % groups, occ_dev)
    my_vals = lax.dynamic_slice_in_dim(own_vals, my_share * rows, rows)

    contract_p = (((0,), (0,)), ((), ()))
    diag = lax.dot_general(own, own, contract_p, precision=PREC,
                           preferred_element_type=jnp.float32)
    diag_share = reduce_scatter_rows(diag, stages, bits)
    diag_amp = diag_share / (my_vals[:, None] + own_vals[None, :])
    diag_full = all_gather_rows(diag_amp, stages, bits)

    up = lax.dot_general(own, above, contract_p, precision=PREC,
                         preferred_element_type=jnp.float32)
    up_share = reduce_scatter_rows(up, stages, bits)
    up_amp = up_share / (my_vals[:, None] + up_vals[None, :])
    prev_amp = passed_along(up_amp, "occ", 1)
    pair_full = all_gather_rows(jnp.stack([up_amp, prev_amp], axis=1), stages, bits)

    contract_b = (((1,), (1,)), ((), ()))
    t_own = lax.dot_general(own, diag_full, contract_b, precision=PREC,
                            preferred_element_type=jnp.float32)
    t_up = lax.dot_general(above, pair_full[:, 0, :], contract_b, precision=PREC,
                           preferred_element_type=jnp.float32)
    t_prev = lax.dot_general(below, pair_full[:, 1, :], (((1,), (0,)), ((), ())),
                             precision=PREC, preferred_element_type=jnp.float32)
    total = t_own + t_up + t_prev
    return (1.3 * total).reshape(aux_dev, occ_dev, virt)


def solution(mesh):
    return jax.shard_map(
        body,
        mesh=mesh,
        in_specs=(P("aux", "occ", None), P(), P()),
        out_specs=P("aux", "occ", None),
        check_vma=False,
    )
```

```python
import jax
import jax.numpy as jnp
import numpy as np
from jax import lax
from jax.sharding import PartitionSpec as P


PREC = lax.Precision.HIGH


def passed_along(value, axis, steps):
    count = lax.axis_size(axis)
    pairs = [(source, (source + steps) % count) for source in range(count)]
    return lax.ppermute(value, axis, pairs)


def pair_values(eps_occ, eps_vir, group, occ_dev):
    occ_part = lax.dynamic_slice_in_dim(eps_occ, group * occ_dev, occ_dev)
    return (occ_part[:, None] - eps_vir[None, :]).reshape(-1)


def aux_stages(count):
    assert count == 16
    stages = []
    core = [(i ^ 1, i & 1) for i in range(count)]
    stages.append(core)

    def x_of(i):
        return (i >> 1) & 3

    def with_x(i, x):
        return (i & ~6) | (x << 1)

    first, second = [], []
    for i in range(count):
        x = x_of(i)
        if i & 1 == 0:
            first.append((with_x(i, x ^ 1), (x & 1) ^ (x >> 1)))
            second.append((with_x(i, 3 - x), x >> 1))
        else:
            first.append((with_x(i, 3 - x), x >> 1))
            second.append((with_x(i, x ^ 1), x & 1))
    stages.append(first)
    stages.append(second)
    stages.append([(i ^ 8, (i >> 3) & 1) for i in range(count)])
    for s, stage in enumerate(stages):
        for i, (j, k) in enumerate(stage):
            assert stage[j][0] == i and stage[j][1] != k
            for t in range(s):
                assert stages[t][i][1] == stages[t][j][1]
    share = [0] * count
    for i in range(count):
        for stage in stages:
            share[i] = share[i] * 2 + stage[i][1]
    assert sorted(share) == list(range(count))
    return stages, share


def keep_bits(stages, share):
    table = np.array([[stage[i][1] for stage in stages] for i in range(len(share))], np.int32)
    idx = lax.axis_index("aux")
    bits = jnp.asarray(table)[idx]
    return [bits[s] for s in range(len(stages))], jnp.asarray(np.array(share, np.int32))[idx]


def reduce_scatter_rows(value, stages, bits):
    for stage, bit in zip(stages, bits):
        half = value.shape[0] // 2
        pairs = [(i, j) for i, (j, _) in enumerate(stage)]
        keep = lax.dynamic_slice_in_dim(value, bit * half, half, 0)
        send = lax.dynamic_slice_in_dim(value, (1 - bit) * half, half, 0)
        value = keep + lax.ppermute(send, "aux", pairs)
    return value


def all_gather_rows(value, stages, bits):
    for stage, bit in reversed(list(zip(stages, bits))):
        rows = value.shape[0]
        pairs = [(i, j) for i, (j, _) in enumerate(stage)]
        got = lax.ppermute(value, "aux", pairs)
        out = jnp.zeros((2 * rows,) + value.shape[1:], value.dtype)
        out = lax.dynamic_update_slice_in_dim(out, value, bit * rows, 0)
        value = lax.dynamic_update_slice_in_dim(out, got, (1 - bit) * rows, 0)
    return value


def body(factors, eps_occ, eps_vir):
    aux_dev, occ_dev, virt = factors.shape
    width = occ_dev * virt
    group = lax.axis_index("occ")
    groups = lax.axis_size("occ")
    aux_count = lax.axis_size("aux")
    stages, share = aux_stages(aux_count)
    bits, my_share = keep_bits(stages, share)
    rows = width // aux_count

    own = factors.reshape(aux_dev, width)
    below = passed_along(factors, "occ", 1).reshape(aux_dev, width)
    above = passed_along(factors, "occ", -1).reshape(aux_dev, width)

    own_vals = pair_values(eps_occ, eps_vir, group, occ_dev)
    up_vals = pair_values(eps_occ, eps_vir, (group + 1) % groups, occ_dev)
    my_vals = lax.dynamic_slice_in_dim(own_vals, my_share * rows, rows)

    contract_p = (((0,), (0,)), ((), ()))
    contract_b = (((1,), (1,)), ((), ()))
    diag = lax.dot_general(own, own, contract_p, precision=PREC,
                           preferred_element_type=jnp.float32)
    diag_share = reduce_scatter_rows(diag, stages, bits)
    diag_amp = diag_share / (my_vals[:, None] + own_vals[None, :])
    diag_full = all_gather_rows(diag_amp, stages, bits)
    t_own = lax.dot_general(own, diag_full, contract_b, precision=PREC,
                            preferred_element_type=jnp.float32)
    above, below, t_own = lax.optimization_barrier((above, below, t_own))

    up = lax.dot_general(own, above, contract_p, precision=PREC,
                         preferred_element_type=jnp.float32)
    up_share = reduce_scatter_rows(up, stages, bits)
    up_amp = up_share / (my_vals[:, None] + up_vals[None, :])
    prev_amp = passed_along(up_amp, "occ", 1)
    up_full = all_gather_rows(up_amp, stages, bits)
    prev_full = all_gather_rows(prev_amp, stages, bits)
    t_up = lax.dot_general(above, up_full, contract_b, precision=PREC,
                           preferred_element_type=jnp.float32)
    t_prev = lax.dot_general(below, prev_full, (((1,), (0,)), ((), ())),
                             precision=PREC, preferred_element_type=jnp.float32)
    total = t_own + t_up + t_prev
    return (1.3 * total).reshape(aux_dev, occ_dev, virt)


def solution(mesh):
    return jax.shard_map(
        body,
        mesh=mesh,
        in_specs=(P("aux", "occ", None), P(), P()),
        out_specs=P("aux", "occ", None),
        check_vma=False,
    )
```

```python
import jax
import jax.numpy as jnp
import numpy as np
from jax import lax
from jax.sharding import PartitionSpec as P


PREC = lax.Precision.HIGH


def passed_along(value, axis, steps):
    count = lax.axis_size(axis)
    pairs = [(source, (source + steps) % count) for source in range(count)]
    return lax.ppermute(value, axis, pairs)


def pair_values(eps_occ, eps_vir, group, occ_dev):
    occ_part = lax.dynamic_slice_in_dim(eps_occ, group * occ_dev, occ_dev)
    return (occ_part[:, None] - eps_vir[None, :]).reshape(-1)


def aux_stages(count):
    assert count == 16
    stages = []
    core = [(i ^ 1, i & 1) for i in range(count)]
    stages.append(core)

    def x_of(i):
        return (i >> 1) & 3

    def with_x(i, x):
        return (i & ~6) | (x << 1)

    first, second = [], []
    for i in range(count):
        x = x_of(i)
        if i & 1 == 0:
            first.append((with_x(i, x ^ 1), (x & 1) ^ (x >> 1)))
            second.append((with_x(i, 3 - x), x >> 1))
        else:
            first.append((with_x(i, 3 - x), x >> 1))
            second.append((with_x(i, x ^ 1), x & 1))
    stages.append(first)
    stages.append(second)
    stages.append([(i ^ 8, (i >> 3) & 1) for i in range(count)])
    for s, stage in enumerate(stages):
        for i, (j, k) in enumerate(stage):
            assert stage[j][0] == i and stage[j][1] != k
            for t in range(s):
                assert stages[t][i][1] == stages[t][j][1]
    share = [0] * count
    for i in range(count):
        for stage in stages:
            share[i] = share[i] * 2 + stage[i][1]
    assert sorted(share) == list(range(count))
    return stages, share


def keep_bits(stages, share):
    table = np.array([[stage[i][1] for stage in stages] for i in range(len(share))], np.int32)
    idx = lax.axis_index("aux")
    bits = jnp.asarray(table)[idx]
    return [bits[s] for s in range(len(stages))], jnp.asarray(np.array(share, np.int32))[idx]


def reduce_scatter_rows(value, stages, bits):
    for stage, bit in zip(stages, bits):
        half = value.shape[0] // 2
        pairs = [(i, j) for i, (j, _) in enumerate(stage)]
        keep = lax.dynamic_slice_in_dim(value, bit * half, half, 0)
        send = lax.dynamic_slice_in_dim(value, (1 - bit) * half, half, 0)
        value = keep + lax.ppermute(send, "aux", pairs)
    return value


def all_gather_rows(value, stages, bits):
    for stage, bit in reversed(list(zip(stages, bits))):
        rows = value.shape[0]
        pairs = [(i, j) for i, (j, _) in enumerate(stage)]
        got = lax.ppermute(value, "aux", pairs)
        out = jnp.zeros((2 * rows,) + value.shape[1:], value.dtype)
        out = lax.dynamic_update_slice_in_dim(out, value, bit * rows, 0)
        value = lax.dynamic_update_slice_in_dim(out, got, (1 - bit) * rows, 0)
    return value


def body(factors, eps_occ, eps_vir):
    aux_dev, occ_dev, virt = factors.shape
    width = occ_dev * virt
    group = lax.axis_index("occ")
    groups = lax.axis_size("occ")
    aux_count = lax.axis_size("aux")
    stages, share = aux_stages(aux_count)
    bits, my_share = keep_bits(stages, share)
    rows = width // aux_count

    own = factors.reshape(aux_dev, width)
    below = passed_along(own, "occ", 1)
    above = passed_along(own, "occ", -1)

    own_vals = pair_values(eps_occ, eps_vir, group, occ_dev)
    up_vals = pair_values(eps_occ, eps_vir, (group + 1) % groups, occ_dev)
    my_vals = lax.dynamic_slice_in_dim(own_vals, my_share * rows, rows)

    contract_p = (((0,), (0,)), ((), ()))
    contract_b = (((1,), (1,)), ((), ()))
    diag = lax.dot_general(own, own, contract_p, precision=PREC,
                           preferred_element_type=jnp.float32)
    diag_share = reduce_scatter_rows(diag, stages, bits)
    diag_amp = diag_share / (my_vals[:, None] + own_vals[None, :])
    above, below, diag_amp = lax.optimization_barrier((above, below, diag_amp))
    diag_full = all_gather_rows(diag_amp, stages, bits)
    t_own = lax.dot_general(own, diag_full, contract_b, precision=PREC,
                            preferred_element_type=jnp.float32)

    up = lax.dot_general(own, above, contract_p, precision=PREC,
                         preferred_element_type=jnp.float32)
    up_share = reduce_scatter_rows(up, stages, bits)
    up_amp = up_share / (my_vals[:, None] + up_vals[None, :])
    prev_amp = passed_along(up_amp, "occ", 1)
    up_full = all_gather_rows(up_amp, stages, bits)
    prev_full = all_gather_rows(prev_amp, stages, bits)
    t_up = lax.dot_general(above, up_full, contract_b, precision=PREC,
                           preferred_element_type=jnp.float32)
    t_prev = lax.dot_general(below, prev_full, (((1,), (0,)), ((), ())),
                             precision=PREC, preferred_element_type=jnp.float32)
    total = t_own + t_up + t_prev
    return (1.3 * total).reshape(aux_dev, occ_dev, virt)


def solution(mesh):
    return jax.shard_map(
        body,
        mesh=mesh,
        in_specs=(P("aux", "occ", None), P(), P()),
        out_specs=P("aux", "occ", None),
        check_vma=False,
    )
```

```python
import jax
import jax.numpy as jnp
import numpy as np
from jax import lax
from jax.sharding import PartitionSpec as P


PREC = lax.Precision.HIGH


def passed_along(value, axis, steps):
    count = lax.axis_size(axis)
    pairs = [(source, (source + steps) % count) for source in range(count)]
    return lax.ppermute(value, axis, pairs)


def pair_values(eps_occ, eps_vir, group, occ_dev):
    occ_part = lax.dynamic_slice_in_dim(eps_occ, group * occ_dev, occ_dev)
    return (occ_part[:, None] - eps_vir[None, :]).reshape(-1)


def aux_stages(count):
    assert count == 16
    stages = []
    core = [(i ^ 1, i & 1) for i in range(count)]
    stages.append(core)

    def x_of(i):
        return (i >> 1) & 3

    def with_x(i, x):
        return (i & ~6) | (x << 1)

    first, second = [], []
    for i in range(count):
        x = x_of(i)
        if i & 1 == 0:
            first.append((with_x(i, x ^ 1), (x & 1) ^ (x >> 1)))
            second.append((with_x(i, 3 - x), x >> 1))
        else:
            first.append((with_x(i, 3 - x), x >> 1))
            second.append((with_x(i, x ^ 1), x & 1))
    stages.append(first)
    stages.append(second)
    stages.append([(i ^ 8, (i >> 3) & 1) for i in range(count)])
    for s, stage in enumerate(stages):
        for i, (j, k) in enumerate(stage):
            assert stage[j][0] == i and stage[j][1] != k
            for t in range(s):
                assert stages[t][i][1] == stages[t][j][1]
    share = [0] * count
    for i in range(count):
        for stage in stages:
            share[i] = share[i] * 2 + stage[i][1]
    assert sorted(share) == list(range(count))
    return stages, share


def keep_bits(stages, share):
    table = np.array([[stage[i][1] for stage in stages] for i in range(len(share))], np.int32)
    idx = lax.axis_index("aux")
    bits = jnp.asarray(table)[idx]
    return [bits[s] for s in range(len(stages))], jnp.asarray(np.array(share, np.int32))[idx]


def reduce_scatter_rows(value, stages, bits):
    for stage, bit in zip(stages, bits):
        half = value.shape[0] // 2
        pairs = [(i, j) for i, (j, _) in enumerate(stage)]
        keep = lax.dynamic_slice_in_dim(value, bit * half, half, 0)
        send = lax.dynamic_slice_in_dim(value, (1 - bit) * half, half, 0)
        value = keep + lax.ppermute(send, "aux", pairs)
    return value


def all_gather_rows(value, stages, bits):
    for stage, bit in reversed(list(zip(stages, bits))):
        rows = value.shape[0]
        pairs = [(i, j) for i, (j, _) in enumerate(stage)]
        got = lax.ppermute(value, "aux", pairs)
        out = jnp.zeros((2 * rows,) + value.shape[1:], value.dtype)
        out = lax.dynamic_update_slice_in_dim(out, value, bit * rows, 0)
        value = lax.dynamic_update_slice_in_dim(out, got, (1 - bit) * rows, 0)
    return value


def body(factors, eps_occ, eps_vir):
    aux_dev, occ_dev, virt = factors.shape
    width = occ_dev * virt
    group = lax.axis_index("occ")
    groups = lax.axis_size("occ")
    aux_count = lax.axis_size("aux")
    stages, share = aux_stages(aux_count)
    bits, my_share = keep_bits(stages, share)
    rows = width // aux_count
    half = aux_dev // 2

    own = factors.reshape(aux_dev, width)
    above_lo = passed_along(factors[:half], "occ", -1).reshape(half, width)
    below_hi = passed_along(factors[half:], "occ", 1).reshape(half, width)

    own_vals = pair_values(eps_occ, eps_vir, group, occ_dev)
    up_vals = pair_values(eps_occ, eps_vir, (group + 1) % groups, occ_dev)
    dn_vals = pair_values(eps_occ, eps_vir, (group + groups - 1) % groups, occ_dev)
    my_vals = lax.dynamic_slice_in_dim(own_vals, my_share * rows, rows)
    my_dn_vals = lax.dynamic_slice_in_dim(dn_vals, my_share * rows, rows)

    contract_p = (((0,), (0,)), ((), ()))
    contract_b = (((1,), (1,)), ((), ()))
    diag = lax.dot_general(own, own, contract_p, precision=PREC,
                           preferred_element_type=jnp.float32)
    diag_share = reduce_scatter_rows(diag, stages, bits)
    diag_amp = diag_share / (my_vals[:, None] + own_vals[None, :])
    above_lo, below_hi, diag_amp, later = lax.optimization_barrier(
        (above_lo, below_hi, diag_amp, factors))
    above_hi = passed_along(later[half:], "occ", -1).reshape(half, width)
    below_lo = passed_along(later[:half], "occ", 1).reshape(half, width)
    diag_full = all_gather_rows(diag_amp, stages, bits)
    t_own = lax.dot_general(own, diag_full, contract_b, precision=PREC,
                            preferred_element_type=jnp.float32)

    up_part = lax.dot_general(own[:half], above_lo, contract_p, precision=PREC,
                              preferred_element_type=jnp.float32)
    dn_part = lax.dot_general(below_hi, own[half:], contract_p, precision=PREC,
                              preferred_element_type=jnp.float32)
    part_share = reduce_scatter_rows(jnp.stack([up_part, dn_part], axis=1), stages, bits)
    up_share = part_share[:, 0] + passed_along(part_share[:, 1], "occ", -1)
    dn_share = part_share[:, 1] + passed_along(part_share[:, 0], "occ", 1)
    up_amp = up_share / (my_vals[:, None] + up_vals[None, :])
    prev_amp = dn_share / (my_dn_vals[:, None] + own_vals[None, :])
    up_full = all_gather_rows(up_amp, stages, bits)
    prev_full = all_gather_rows(prev_amp, stages, bits)
    contract_a = (((1,), (0,)), ((), ()))
    pieces = []
    for above, below, own_rows in ((above_lo, below_lo, t_own[:half]),
                                    (above_hi, below_hi, t_own[half:])):
        t_up = lax.dot_general(above, up_full, contract_b, precision=PREC,
                               preferred_element_type=jnp.float32)
        t_prev = lax.dot_general(below, prev_full, contract_a, precision=PREC,
                                 preferred_element_type=jnp.float32)
        pieces.append(own_rows + t_up + t_prev)
    total = jnp.concatenate(pieces, axis=0)
    return (1.3 * total).reshape(aux_dev, occ_dev, virt)


def solution(mesh):
    return jax.shard_map(
        body,
        mesh=mesh,
        in_specs=(P("aux", "occ", None), P(), P()),
        out_specs=P("aux", "occ", None),
        check_vma=False,
    )
```

```python
import jax
import jax.numpy as jnp
import numpy as np
from jax import lax
from jax.sharding import PartitionSpec as P


PREC = lax.Precision.HIGH


def passed_along(value, axis, steps):
    count = lax.axis_size(axis)
    pairs = [(source, (source + steps) % count) for source in range(count)]
    return lax.ppermute(value, axis, pairs)


def pair_values(eps_occ, eps_vir, group, occ_dev):
    occ_part = lax.dynamic_slice_in_dim(eps_occ, group * occ_dev, occ_dev)
    return (occ_part[:, None] - eps_vir[None, :]).reshape(-1)


def aux_stages(count):
    assert count == 16
    stages = []
    core = [(i ^ 1, i & 1) for i in range(count)]
    stages.append(core)

    def x_of(i):
        return (i >> 1) & 3

    def with_x(i, x):
        return (i & ~6) | (x << 1)

    first, second = [], []
    for i in range(count):
        x = x_of(i)
        if i & 1 == 0:
            first.append((with_x(i, x ^ 1), (x & 1) ^ (x >> 1)))
            second.append((with_x(i, 3 - x), x >> 1))
        else:
            first.append((with_x(i, 3 - x), x >> 1))
            second.append((with_x(i, x ^ 1), x & 1))
    stages.append(first)
    stages.append(second)
    stages.append([(i ^ 8, (i >> 3) & 1) for i in range(count)])
    for s, stage in enumerate(stages):
        for i, (j, k) in enumerate(stage):
            assert stage[j][0] == i and stage[j][1] != k
            for t in range(s):
                assert stages[t][i][1] == stages[t][j][1]
    share = [0] * count
    for i in range(count):
        for stage in stages:
            share[i] = share[i] * 2 + stage[i][1]
    assert sorted(share) == list(range(count))
    return stages, share


def keep_bits(stages, share):
    table = np.array([[stage[i][1] for stage in stages] for i in range(len(share))], np.int32)
    idx = lax.axis_index("aux")
    bits = jnp.asarray(table)[idx]
    return [bits[s] for s in range(len(stages))], jnp.asarray(np.array(share, np.int32))[idx]


def reduce_scatter_a2a(value, count):
    chunks = value.reshape((count, value.shape[0] // count) + value.shape[1:])
    got = lax.all_to_all(chunks, "aux", 0, 0, tiled=False)
    return got.sum(axis=0)


def all_gather_a2a(value, count):
    tiles = jnp.broadcast_to(value[None], (count,) + value.shape)
    got = lax.all_to_all(tiles, "aux", 0, 0, tiled=False)
    return got.reshape((count * value.shape[0],) + value.shape[1:])


def body(factors, eps_occ, eps_vir):
    aux_dev, occ_dev, virt = factors.shape
    width = occ_dev * virt
    group = lax.axis_index("occ")
    groups = lax.axis_size("occ")
    aux_count = lax.axis_size("aux")
    stages, share = aux_stages(aux_count)
    _, my_share = keep_bits(stages, share)
    my_share = lax.axis_index("aux")
    rows = width // aux_count

    own = factors.reshape(aux_dev, width)
    below = passed_along(factors, "occ", 1).reshape(aux_dev, width)
    above = passed_along(factors, "occ", -1).reshape(aux_dev, width)

    own_vals = pair_values(eps_occ, eps_vir, group, occ_dev)
    up_vals = pair_values(eps_occ, eps_vir, (group + 1) % groups, occ_dev)
    my_vals = lax.dynamic_slice_in_dim(own_vals, my_share * rows, rows)

    contract_p = (((0,), (0,)), ((), ()))
    contract_b = (((1,), (1,)), ((), ()))
    diag = lax.dot_general(own, own, contract_p, precision=PREC,
                           preferred_element_type=jnp.float32)
    diag_share = reduce_scatter_a2a(diag, aux_count)
    diag_amp = diag_share / (my_vals[:, None] + own_vals[None, :])
    above, below, diag_amp = lax.optimization_barrier((above, below, diag_amp))
    diag_full = all_gather_a2a(diag_amp, aux_count)
    t_own = lax.dot_general(own, diag_full, contract_b, precision=PREC,
                            preferred_element_type=jnp.float32)

    up = lax.dot_general(own, above, contract_p, precision=PREC,
                         preferred_element_type=jnp.float32)
    up_share = reduce_scatter_a2a(up, aux_count)
    up_amp = up_share / (my_vals[:, None] + up_vals[None, :])
    prev_amp = passed_along(up_amp, "occ", 1)
    up_full = all_gather_a2a(up_amp, aux_count)
    prev_full = all_gather_a2a(prev_amp, aux_count)
    t_up = lax.dot_general(above, up_full, contract_b, precision=PREC,
                           preferred_element_type=jnp.float32)
    t_prev = lax.dot_general(below, prev_full, (((1,), (0,)), ((), ())),
                             precision=PREC, preferred_element_type=jnp.float32)
    total = t_own + t_up + t_prev
    return (1.3 * total).reshape(aux_dev, occ_dev, virt)


def solution(mesh):
    return jax.shard_map(
        body,
        mesh=mesh,
        in_specs=(P("aux", "occ", None), P(), P()),
        out_specs=P("aux", "occ", None),
        check_vma=False,
    )
```

```python
import jax
import jax.numpy as jnp
import numpy as np
from jax import lax
from jax.sharding import PartitionSpec as P


PREC = lax.Precision.HIGH


def passed_along(value, axis, steps):
    count = lax.axis_size(axis)
    pairs = [(source, (source + steps) % count) for source in range(count)]
    return lax.ppermute(value, axis, pairs)


def pair_values(eps_occ, eps_vir, group, occ_dev):
    occ_part = lax.dynamic_slice_in_dim(eps_occ, group * occ_dev, occ_dev)
    return (occ_part[:, None] - eps_vir[None, :]).reshape(-1)


def aux_stages(count):
    assert count == 16
    stages = []
    core = [(i ^ 1, i & 1) for i in range(count)]
    stages.append(core)

    def x_of(i):
        return (i >> 1) & 3

    def with_x(i, x):
        return (i & ~6) | (x << 1)

    first, second = [], []
    for i in range(count):
        x = x_of(i)
        if i & 1 == 0:
            first.append((with_x(i, x ^ 1), (x & 1) ^ (x >> 1)))
            second.append((with_x(i, 3 - x), x >> 1))
        else:
            first.append((with_x(i, 3 - x), x >> 1))
            second.append((with_x(i, x ^ 1), x & 1))
    stages.append(first)
    stages.append(second)
    stages.append([(i ^ 8, (i >> 3) & 1) for i in range(count)])
    for s, stage in enumerate(stages):
        for i, (j, k) in enumerate(stage):
            assert stage[j][0] == i and stage[j][1] != k
            for t in range(s):
                assert stages[t][i][1] == stages[t][j][1]
    share = [0] * count
    for i in range(count):
        for stage in stages:
            share[i] = share[i] * 2 + stage[i][1]
    assert sorted(share) == list(range(count))
    return stages, share


def keep_bits(stages, share):
    table = np.array([[stage[i][1] for stage in stages] for i in range(len(share))], np.int32)
    idx = lax.axis_index("aux")
    bits = jnp.asarray(table)[idx]
    return [bits[s] for s in range(len(stages))], jnp.asarray(np.array(share, np.int32))[idx]


def reduce_scatter_rows(value, stages, bits, last_parts=False):
    for n, (stage, bit) in enumerate(zip(stages, bits)):
        half = value.shape[0] // 2
        pairs = [(i, j) for i, (j, _) in enumerate(stage)]
        keep = lax.dynamic_slice_in_dim(value, bit * half, half, 0)
        send = lax.dynamic_slice_in_dim(value, (1 - bit) * half, half, 0)
        if last_parts and n == len(stages) - 1:
            return keep, send, pairs
        value = keep + lax.ppermute(send, "aux", pairs)
    return value


def all_gather_rows(value, stages, bits):
    for stage, bit in reversed(list(zip(stages, bits))):
        rows = value.shape[0]
        pairs = [(i, j) for i, (j, _) in enumerate(stage)]
        got = lax.ppermute(value, "aux", pairs)
        out = jnp.zeros((2 * rows,) + value.shape[1:], value.dtype)
        out = lax.dynamic_update_slice_in_dim(out, value, bit * rows, 0)
        value = lax.dynamic_update_slice_in_dim(out, got, (1 - bit) * rows, 0)
    return value


def body(factors, eps_occ, eps_vir):
    aux_dev, occ_dev, virt = factors.shape
    width = occ_dev * virt
    group = lax.axis_index("occ")
    groups = lax.axis_size("occ")
    aux_count = lax.axis_size("aux")
    stages, share = aux_stages(aux_count)
    bits, my_share = keep_bits(stages, share)
    rows = width // aux_count

    own = factors.reshape(aux_dev, width)
    below = passed_along(factors, "occ", 1).reshape(aux_dev, width)
    above = passed_along(factors, "occ", -1).reshape(aux_dev, width)

    own_vals = pair_values(eps_occ, eps_vir, group, occ_dev)
    up_vals = pair_values(eps_occ, eps_vir, (group + 1) % groups, occ_dev)
    my_vals = lax.dynamic_slice_in_dim(own_vals, my_share * rows, rows)
    dn_vals = pair_values(eps_occ, eps_vir, (group + groups - 1) % groups, occ_dev)
    my_dn_vals = lax.dynamic_slice_in_dim(dn_vals, my_share * rows, rows)

    contract_p = (((0,), (0,)), ((), ()))
    contract_b = (((1,), (1,)), ((), ()))
    diag = lax.dot_general(own, own, contract_p, precision=PREC,
                           preferred_element_type=jnp.float32)
    diag_share = reduce_scatter_rows(diag, stages, bits)
    diag_amp = diag_share / (my_vals[:, None] + own_vals[None, :])
    above, below, diag_amp = lax.optimization_barrier((above, below, diag_amp))
    diag_full = all_gather_rows(diag_amp, stages, bits)
    t_own = lax.dot_general(own, diag_full, contract_b, precision=PREC,
                            preferred_element_type=jnp.float32)

    up = lax.dot_general(own, above, contract_p, precision=PREC,
                         preferred_element_type=jnp.float32)
    keep, send, last = reduce_scatter_rows(up, stages, bits, last_parts=True)
    up_share = keep + lax.ppermute(send, "aux", last)
    across = [(g * aux_count + i, ((g + 1) % groups) * aux_count + j)
              for g in range(groups) for i, j in last]
    prev_share = passed_along(keep, "occ", 1) + lax.ppermute(send, ("occ", "aux"), across)
    up_amp = up_share / (my_vals[:, None] + up_vals[None, :])
    prev_amp = prev_share / (my_dn_vals[:, None] + own_vals[None, :])
    pair_full = all_gather_rows(jnp.stack([up_amp, prev_amp], axis=1), stages, bits)
    t_up = lax.dot_general(above, pair_full[:, 0], contract_b, precision=PREC,
                           preferred_element_type=jnp.float32)
    t_prev = lax.dot_general(below, pair_full[:, 1], (((1,), (0,)), ((), ())),
                             precision=PREC, preferred_element_type=jnp.float32)
    total = t_own + t_up + t_prev
    return (1.3 * total).reshape(aux_dev, occ_dev, virt)


def solution(mesh):
    return jax.shard_map(
        body,
        mesh=mesh,
        in_specs=(P("aux", "occ", None), P(), P()),
        out_specs=P("aux", "occ", None),
        check_vma=False,
    )
```

```python
import jax
import jax.numpy as jnp
import numpy as np
from jax import lax
from jax.sharding import PartitionSpec as P


PREC = lax.Precision.HIGH


def passed_along(value, axis, steps):
    count = lax.axis_size(axis)
    pairs = [(source, (source + steps) % count) for source in range(count)]
    return lax.ppermute(value, axis, pairs)


def pair_values(eps_occ, eps_vir, group, occ_dev):
    occ_part = lax.dynamic_slice_in_dim(eps_occ, group * occ_dev, occ_dev)
    return (occ_part[:, None] - eps_vir[None, :]).reshape(-1)


def aux_stages(count):
    assert count == 16
    stages = []
    core = [(i ^ 1, i & 1) for i in range(count)]
    stages.append(core)

    def x_of(i):
        return (i >> 1) & 3

    def with_x(i, x):
        return (i & ~6) | (x << 1)

    first, second = [], []
    for i in range(count):
        x = x_of(i)
        if i & 1 == 0:
            first.append((with_x(i, x ^ 1), (x & 1) ^ (x >> 1)))
            second.append((with_x(i, 3 - x), x >> 1))
        else:
            first.append((with_x(i, 3 - x), x >> 1))
            second.append((with_x(i, x ^ 1), x & 1))
    stages.append(first)
    stages.append(second)
    stages.append([(i ^ 8, (i >> 3) & 1) for i in range(count)])
    for s, stage in enumerate(stages):
        for i, (j, k) in enumerate(stage):
            assert stage[j][0] == i and stage[j][1] != k
            for t in range(s):
                assert stages[t][i][1] == stages[t][j][1]
    share = [0] * count
    for i in range(count):
        for stage in stages:
            share[i] = share[i] * 2 + stage[i][1]
    assert sorted(share) == list(range(count))
    return stages, share


def keep_bits(stages, share):
    table = np.array([[stage[i][1] for stage in stages] for i in range(len(share))], np.int32)
    idx = lax.axis_index("aux")
    bits = jnp.asarray(table)[idx]
    return [bits[s] for s in range(len(stages))], jnp.asarray(np.array(share, np.int32))[idx]


def reduce_scatter_rows(value, stages, bits, last_parts=False):
    for n, (stage, bit) in enumerate(zip(stages, bits)):
        half = value.shape[0] // 2
        pairs = [(i, j) for i, (j, _) in enumerate(stage)]
        keep = lax.dynamic_slice_in_dim(value, bit * half, half, 0)
        send = lax.dynamic_slice_in_dim(value, (1 - bit) * half, half, 0)
        if last_parts and n == len(stages) - 1:
            return keep, send, pairs
        value = keep + lax.ppermute(send, "aux", pairs)
    return value


def all_gather_rows(value, stages, bits):
    for stage, bit in reversed(list(zip(stages, bits))):
        rows = value.shape[0]
        pairs = [(i, j) for i, (j, _) in enumerate(stage)]
        got = lax.ppermute(value, "aux", pairs)
        out = jnp.zeros((2 * rows,) + value.shape[1:], value.dtype)
        out = lax.dynamic_update_slice_in_dim(out, value, bit * rows, 0)
        value = lax.dynamic_update_slice_in_dim(out, got, (1 - bit) * rows, 0)
    return value


def body(factors, eps_occ, eps_vir):
    aux_dev, occ_dev, virt = factors.shape
    width = occ_dev * virt
    group = lax.axis_index("occ")
    groups = lax.axis_size("occ")
    aux_count = lax.axis_size("aux")
    stages, share = aux_stages(aux_count)
    bits, my_share = keep_bits(stages, share)
    rows = width // aux_count

    own = factors.reshape(aux_dev, width)
    below = passed_along(factors, "occ", 1).reshape(aux_dev, width)
    above = passed_along(factors, "occ", -1).reshape(aux_dev, width)

    own_vals = pair_values(eps_occ, eps_vir, group, occ_dev)
    up_vals = pair_values(eps_occ, eps_vir, (group + 1) % groups, occ_dev)
    my_vals = lax.dynamic_slice_in_dim(own_vals, my_share * rows, rows)
    dn_vals = pair_values(eps_occ, eps_vir, (group + groups - 1) % groups, occ_dev)
    my_dn_vals = lax.dynamic_slice_in_dim(dn_vals, my_share * rows, rows)

    contract_p = (((0,), (0,)), ((), ()))
    contract_b = (((1,), (1,)), ((), ()))
    diag = lax.dot_general(own, own, contract_p, precision=PREC,
                           preferred_element_type=jnp.float32)
    diag_share = reduce_scatter_rows(diag, stages, bits)
    diag_amp = diag_share / (my_vals[:, None] + own_vals[None, :])
    above, below, diag_amp = lax.optimization_barrier((above, below, diag_amp))
    diag_full = all_gather_rows(diag_amp, stages, bits)
    t_own = lax.dot_general(own, diag_full, contract_b, precision=PREC,
                            preferred_element_type=jnp.float32)

    up = lax.dot_general(own, above, contract_p, precision=PREC,
                         preferred_element_type=jnp.float32)
    keep, send, last = reduce_scatter_rows(up, stages, bits, last_parts=True)
    up_share = keep + lax.ppermute(send, "aux", last)
    across = [(g * aux_count + i, ((g + 1) % groups) * aux_count + j)
              for g in range(groups) for i, j in last]
    prev_share = passed_along(keep, "occ", 1) + lax.ppermute(send, ("occ", "aux"), across)
    up_amp = up_share / (my_vals[:, None] + up_vals[None, :])
    prev_amp = prev_share / (my_dn_vals[:, None] + own_vals[None, :])
    up_full = all_gather_rows(up_amp, stages, bits)
    prev_full = all_gather_rows(prev_amp, stages, bits)
    t_up = lax.dot_general(above, up_full, contract_b, precision=PREC,
                           preferred_element_type=jnp.float32)
    t_prev = lax.dot_general(below, prev_full, (((1,), (0,)), ((), ())),
                             precision=PREC, preferred_element_type=jnp.float32)
    total = t_own + t_up + t_prev
    return (1.3 * total).reshape(aux_dev, occ_dev, virt)


def solution(mesh):
    return jax.shard_map(
        body,
        mesh=mesh,
        in_specs=(P("aux", "occ", None), P(), P()),
        out_specs=P("aux", "occ", None),
        check_vma=False,
    )
```

```python
import jax
import jax.numpy as jnp
import numpy as np
from jax import lax
from jax.sharding import PartitionSpec as P


PREC = lax.Precision.HIGH


def passed_along(value, axis, steps):
    count = lax.axis_size(axis)
    pairs = [(source, (source + steps) % count) for source in range(count)]
    return lax.ppermute(value, axis, pairs)


def pair_values(eps_occ, eps_vir, group, occ_dev):
    occ_part = lax.dynamic_slice_in_dim(eps_occ, group * occ_dev, occ_dev)
    return (occ_part[:, None] - eps_vir[None, :]).reshape(-1)


def aux_stages(count):
    assert count == 16
    stages = []
    core = [(i ^ 1, i & 1) for i in range(count)]
    stages.append(core)

    def x_of(i):
        return (i >> 1) & 3

    def with_x(i, x):
        return (i & ~6) | (x << 1)

    first, second = [], []
    for i in range(count):
        x = x_of(i)
        if i & 1 == 0:
            first.append((with_x(i, x ^ 1), (x & 1) ^ (x >> 1)))
            second.append((with_x(i, 3 - x), x >> 1))
        else:
            first.append((with_x(i, 3 - x), x >> 1))
            second.append((with_x(i, x ^ 1), x & 1))
    stages.append(first)
    stages.append(second)
    stages.append([(i ^ 8, (i >> 3) & 1) for i in range(count)])
    for s, stage in enumerate(stages):
        for i, (j, k) in enumerate(stage):
            assert stage[j][0] == i and stage[j][1] != k
            for t in range(s):
                assert stages[t][i][1] == stages[t][j][1]
    share = [0] * count
    for i in range(count):
        for stage in stages:
            share[i] = share[i] * 2 + stage[i][1]
    assert sorted(share) == list(range(count))
    return stages, share


def keep_bits(stages, share):
    table = np.array([[stage[i][1] for stage in stages] for i in range(len(share))], np.int32)
    idx = lax.axis_index("aux")
    bits = jnp.asarray(table)[idx]
    return [bits[s] for s in range(len(stages))], jnp.asarray(np.array(share, np.int32))[idx]


def reduce_scatter_rows(value, stages, bits):
    for stage, bit in zip(stages, bits):
        half = value.shape[0] // 2
        pairs = [(i, j) for i, (j, _) in enumerate(stage)]
        keep = lax.dynamic_slice_in_dim(value, bit * half, half, 0)
        send = lax.dynamic_slice_in_dim(value, (1 - bit) * half, half, 0)
        value = keep + lax.ppermute(send, "aux", pairs)
    return value


def all_gather_rows(value, stages, bits):
    for stage, bit in reversed(list(zip(stages, bits))):
        rows = value.shape[0]
        pairs = [(i, j) for i, (j, _) in enumerate(stage)]
        got = lax.ppermute(value, "aux", pairs)
        out = jnp.zeros((2 * rows,) + value.shape[1:], value.dtype)
        out = lax.dynamic_update_slice_in_dim(out, value, bit * rows, 0)
        value = lax.dynamic_update_slice_in_dim(out, got, (1 - bit) * rows, 0)
    return value


def body(factors, eps_occ, eps_vir):
    _, occ_dev, virt = factors.shape
    width = occ_dev * virt
    group = lax.axis_index("occ")
    groups = lax.axis_size("occ")
    aux_count = lax.axis_size("aux")
    stages, share = aux_stages(aux_count)
    bits, my_share = keep_bits(stages, share)
    rows = width // aux_count

    below = passed_along(factors, "occ", 1)
    above = passed_along(factors, "occ", -1)

    own_vals = pair_values(eps_occ, eps_vir, group, occ_dev)
    up_vals = pair_values(eps_occ, eps_vir, (group + 1) % groups, occ_dev)
    my_vals = lax.dynamic_slice_in_dim(own_vals, my_share * rows, rows)

    contract_p = (((0, 1), (0, 1)), ((), ()))
    contract_b = (((2,), (1,)), ((), ()))
    diag = lax.dot_general(factors, factors, contract_p, precision=PREC,
                           preferred_element_type=jnp.float32)
    diag_share = reduce_scatter_rows(diag, stages, bits)
    diag_amp = diag_share / (my_vals[:, None] + own_vals[None, :])
    above, below, diag_amp = lax.optimization_barrier((above, below, diag_amp))
    diag_full = all_gather_rows(diag_amp, stages, bits)
    t_own = lax.dot_general(factors, diag_full, contract_b, precision=PREC,
                            preferred_element_type=jnp.float32)

    up = lax.dot_general(factors, above, contract_p, precision=PREC,
                         preferred_element_type=jnp.float32)
    up_share = reduce_scatter_rows(up, stages, bits)
    up_amp = up_share / (my_vals[:, None] + up_vals[None, :])
    prev_amp = passed_along(up_amp, "occ", 1)
    up_full = all_gather_rows(up_amp, stages, bits)
    prev_full = all_gather_rows(prev_amp, stages, bits)
    t_up = lax.dot_general(above, up_full, contract_b, precision=PREC,
                           preferred_element_type=jnp.float32)
    t_prev = lax.dot_general(below, prev_full, (((2,), (0,)), ((), ())),
                             precision=PREC, preferred_element_type=jnp.float32)
    total = t_own + t_up + t_prev
    return 1.3 * total


def solution(mesh):
    return jax.shard_map(
        body,
        mesh=mesh,
        in_specs=(P("aux", "occ", None), P(), P()),
        out_specs=P("aux", "occ", None),
        check_vma=False,
    )
```

```python
import jax
import jax.numpy as jnp
import numpy as np
from jax import lax
from jax.sharding import PartitionSpec as P


PREC = lax.Precision.HIGH


def passed_along(value, axis, steps):
    count = lax.axis_size(axis)
    pairs = [(source, (source + steps) % count) for source in range(count)]
    return lax.ppermute(value, axis, pairs)


def pair_values(eps_occ, eps_vir, group, occ_dev):
    occ_part = lax.dynamic_slice_in_dim(eps_occ, group * occ_dev, occ_dev)
    return (occ_part[:, None] - eps_vir[None, :]).reshape(-1)


def aux_stages(count):
    assert count == 16
    stages = []
    core = [(i ^ 1, i & 1) for i in range(count)]
    stages.append(core)

    def x_of(i):
        return (i >> 1) & 3

    def with_x(i, x):
        return (i & ~6) | (x << 1)

    first, second = [], []
    for i in range(count):
        x = x_of(i)
        if i & 1 == 0:
            first.append((with_x(i, x ^ 1), (x & 1) ^ (x >> 1)))
            second.append((with_x(i, 3 - x), x >> 1))
        else:
            first.append((with_x(i, 3 - x), x >> 1))
            second.append((with_x(i, x ^ 1), x & 1))
    stages.append(first)
    stages.append(second)
    stages.append([(i ^ 8, (i >> 3) & 1) for i in range(count)])
    for s, stage in enumerate(stages):
        for i, (j, k) in enumerate(stage):
            assert stage[j][0] == i and stage[j][1] != k
            for t in range(s):
                assert stages[t][i][1] == stages[t][j][1]
    share = [0] * count
    for i in range(count):
        for stage in stages:
            share[i] = share[i] * 2 + stage[i][1]
    assert sorted(share) == list(range(count))
    return stages, share


def keep_bits(stages, share):
    table = np.array([[stage[i][1] for stage in stages] for i in range(len(share))], np.int32)
    idx = lax.axis_index("aux")
    bits = jnp.asarray(table)[idx]
    return [bits[s] for s in range(len(stages))], jnp.asarray(np.array(share, np.int32))[idx]


def reduce_scatter_rows(value, stages, bits):
    for stage, bit in zip(stages, bits):
        half = value.shape[0] // 2
        pairs = [(i, j) for i, (j, _) in enumerate(stage)]
        keep = lax.dynamic_slice_in_dim(value, bit * half, half, 0)
        send = lax.dynamic_slice_in_dim(value, (1 - bit) * half, half, 0)
        value = keep + lax.ppermute(send, "aux", pairs)
    return value


def all_gather_rows(value, stages, bits):
    for stage, bit in reversed(list(zip(stages, bits))):
        rows = value.shape[0]
        pairs = [(i, j) for i, (j, _) in enumerate(stage)]
        got = lax.ppermute(value, "aux", pairs)
        out = jnp.zeros((2 * rows,) + value.shape[1:], value.dtype)
        out = lax.dynamic_update_slice_in_dim(out, value, bit * rows, 0)
        value = lax.dynamic_update_slice_in_dim(out, got, (1 - bit) * rows, 0)
    return value


def body(factors, eps_occ, eps_vir):
    aux_dev, occ_dev, virt = factors.shape
    width = occ_dev * virt
    group = lax.axis_index("occ")
    groups = lax.axis_size("occ")
    aux_count = lax.axis_size("aux")
    stages, share = aux_stages(aux_count)
    bits, my_share = keep_bits(stages, share)
    rows = width // aux_count

    own = factors.reshape(aux_dev, width)
    half = aux_dev // 2
    below = jnp.concatenate([passed_along(factors[:half], "occ", 1),
                             passed_along(factors[half:], "occ", 1)]).reshape(aux_dev, width)
    above = jnp.concatenate([passed_along(factors[:half], "occ", -1),
                             passed_along(factors[half:], "occ", -1)]).reshape(aux_dev, width)

    own_vals = pair_values(eps_occ, eps_vir, group, occ_dev)
    up_vals = pair_values(eps_occ, eps_vir, (group + 1) % groups, occ_dev)
    my_vals = lax.dynamic_slice_in_dim(own_vals, my_share * rows, rows)

    contract_p = (((0,), (0,)), ((), ()))
    contract_b = (((1,), (1,)), ((), ()))
    diag = lax.dot_general(own, own, contract_p, precision=PREC,
                           preferred_element_type=jnp.float32)
    diag_share = reduce_scatter_rows(diag, stages, bits)
    diag_amp = diag_share / (my_vals[:, None] + own_vals[None, :])
    above, below, diag_amp = lax.optimization_barrier((above, below, diag_amp))
    diag_full = all_gather_rows(diag_amp, stages, bits)
    t_own = lax.dot_general(own, diag_full, contract_b, precision=PREC,
                            preferred_element_type=jnp.float32)

    up = lax.dot_general(own, above, contract_p, precision=PREC,
                         preferred_element_type=jnp.float32)
    up_share = reduce_scatter_rows(up, stages, bits)
    up_amp = up_share / (my_vals[:, None] + up_vals[None, :])
    prev_amp = passed_along(up_amp, "occ", 1)
    up_full = all_gather_rows(up_amp, stages, bits)
    prev_full = all_gather_rows(prev_amp, stages, bits)
    t_up = lax.dot_general(above, up_full, contract_b, precision=PREC,
                           preferred_element_type=jnp.float32)
    t_prev = lax.dot_general(below, prev_full, (((1,), (0,)), ((), ())),
                             precision=PREC, preferred_element_type=jnp.float32)
    total = t_own + t_up + t_prev
    return (1.3 * total).reshape(aux_dev, occ_dev, virt)


def solution(mesh):
    return jax.shard_map(
        body,
        mesh=mesh,
        in_specs=(P("aux", "occ", None), P(), P()),
        out_specs=P("aux", "occ", None),
        check_vma=False,
    )
```

```python
import jax
import jax.numpy as jnp
import numpy as np
from jax import lax
from jax.sharding import PartitionSpec as P


PREC = lax.Precision.HIGH


def passed_along(value, axis, steps):
    count = lax.axis_size(axis)
    pairs = [(source, (source + steps) % count) for source in range(count)]
    return lax.ppermute(value, axis, pairs)


def pair_values(eps_occ, eps_vir, group, occ_dev):
    occ_part = lax.dynamic_slice_in_dim(eps_occ, group * occ_dev, occ_dev)
    return (occ_part[:, None] - eps_vir[None, :]).reshape(-1)


def aux_stages(count):
    assert count == 16
    stages = []
    core = [(i ^ 1, i & 1) for i in range(count)]
    stages.append(core)

    def x_of(i):
        return (i >> 1) & 3

    def with_x(i, x):
        return (i & ~6) | (x << 1)

    first, second = [], []
    for i in range(count):
        x = x_of(i)
        if i & 1 == 0:
            first.append((with_x(i, x ^ 1), (x & 1) ^ (x >> 1)))
            second.append((with_x(i, 3 - x), x >> 1))
        else:
            first.append((with_x(i, 3 - x), x >> 1))
            second.append((with_x(i, x ^ 1), x & 1))
    stages.append(first)
    stages.append(second)
    stages.append([(i ^ 8, (i >> 3) & 1) for i in range(count)])
    for s, stage in enumerate(stages):
        for i, (j, k) in enumerate(stage):
            assert stage[j][0] == i and stage[j][1] != k
            for t in range(s):
                assert stages[t][i][1] == stages[t][j][1]
    share = [0] * count
    for i in range(count):
        for stage in stages:
            share[i] = share[i] * 2 + stage[i][1]
    assert sorted(share) == list(range(count))
    return stages, share


def keep_bits(stages, share):
    table = np.array([[stage[i][1] for stage in stages] for i in range(len(share))], np.int32)
    idx = lax.axis_index("aux")
    bits = jnp.asarray(table)[idx]
    return [bits[s] for s in range(len(stages))], jnp.asarray(np.array(share, np.int32))[idx]


def reduce_scatter_rows(value, stages, bits):
    for stage, bit in zip(stages, bits):
        half = value.shape[0] // 2
        pairs = [(i, j) for i, (j, _) in enumerate(stage)]
        keep = lax.dynamic_slice_in_dim(value, bit * half, half, 0)
        send = lax.dynamic_slice_in_dim(value, (1 - bit) * half, half, 0)
        value = keep + lax.ppermute(send, "aux", pairs)
    return value


def all_gather_rows(value, stages, bits):
    for stage, bit in reversed(list(zip(stages, bits))):
        rows = value.shape[0]
        pairs = [(i, j) for i, (j, _) in enumerate(stage)]
        got = lax.ppermute(value, "aux", pairs)
        out = jnp.zeros((2 * rows,) + value.shape[1:], value.dtype)
        out = lax.dynamic_update_slice_in_dim(out, value, bit * rows, 0)
        value = lax.dynamic_update_slice_in_dim(out, got, (1 - bit) * rows, 0)
    return value


def body(factors, eps_occ, eps_vir):
    aux_dev, occ_dev, virt = factors.shape
    width = occ_dev * virt
    group = lax.axis_index("occ")
    groups = lax.axis_size("occ")
    aux_count = lax.axis_size("aux")
    stages, share = aux_stages(aux_count)
    bits, my_share = keep_bits(stages, share)
    rows = width // aux_count

    own = factors.reshape(aux_dev, width)
    below = passed_along(factors, "occ", 1).reshape(aux_dev, width)
    above = passed_along(factors, "occ", -1).reshape(aux_dev, width)

    own_vals = pair_values(eps_occ, eps_vir, group, occ_dev)
    up_vals = pair_values(eps_occ, eps_vir, (group + 1) % groups, occ_dev)
    my_vals = lax.dynamic_slice_in_dim(own_vals, my_share * rows, rows)

    contract_p = (((0,), (0,)), ((), ()))
    contract_b = (((1,), (1,)), ((), ()))
    diag = lax.dot_general(own, own, contract_p, precision=PREC,
                           preferred_element_type=jnp.float32)
    diag_share = reduce_scatter_rows(diag, stages, bits)
    diag_amp = diag_share / (my_vals[:, None] + own_vals[None, :])
    above, below, diag_amp = lax.optimization_barrier((above, below, diag_amp))
    diag_full = all_gather_rows(diag_amp, stages, bits)
    t_own = lax.dot_general(own, diag_full, contract_b, precision=PREC,
                            preferred_element_type=jnp.float32)

    up = lax.dot_general(own, above, contract_p, precision=PREC,
                         preferred_element_type=jnp.float32)
    up_share = reduce_scatter_rows(up, stages, bits)
    up_amp = up_share / (my_vals[:, None] + up_vals[None, :])
    z_pairs = [(i, j) for i, (j, _) in enumerate(stages[-1])]
    across = [(g * aux_count + i, ((g + 1) % groups) * aux_count + j)
              for g in range(groups) for i, j in z_pairs]
    prev_mine = passed_along(up_amp, "occ", 1)
    prev_pair = lax.ppermute(up_amp, ("occ", "aux"), across)
    prev_two = jnp.zeros((2 * rows,) + up_amp.shape[1:], up_amp.dtype)
    prev_two = lax.dynamic_update_slice_in_dim(prev_two, prev_mine, bits[-1] * rows, 0)
    prev_two = lax.dynamic_update_slice_in_dim(prev_two, prev_pair, (1 - bits[-1]) * rows, 0)
    up_full = all_gather_rows(up_amp, stages, bits)
    prev_full = all_gather_rows(prev_two, stages[:-1], bits[:-1])
    t_up = lax.dot_general(above, up_full, contract_b, precision=PREC,
                           preferred_element_type=jnp.float32)
    t_prev = lax.dot_general(below, prev_full, (((1,), (0,)), ((), ())),
                             precision=PREC, preferred_element_type=jnp.float32)
    total = t_own + t_up + t_prev
    return (1.3 * total).reshape(aux_dev, occ_dev, virt)


def solution(mesh):
    return jax.shard_map(
        body,
        mesh=mesh,
        in_specs=(P("aux", "occ", None), P(), P()),
        out_specs=P("aux", "occ", None),
        check_vma=False,
    )
```

```python
import jax
import jax.numpy as jnp
import numpy as np
from jax import lax
from jax.sharding import PartitionSpec as P


PREC = lax.Precision.HIGH


def passed_along(value, axis, steps):
    count = lax.axis_size(axis)
    pairs = [(source, (source + steps) % count) for source in range(count)]
    return lax.ppermute(value, axis, pairs)


def pair_values(eps_occ, eps_vir, group, occ_dev):
    occ_part = lax.dynamic_slice_in_dim(eps_occ, group * occ_dev, occ_dev)
    return (occ_part[:, None] - eps_vir[None, :]).reshape(-1)


def aux_stages(count):
    assert count == 16
    stages = []
    core = [(i ^ 1, i & 1) for i in range(count)]
    stages.append(core)

    def x_of(i):
        return (i >> 1) & 3

    def with_x(i, x):
        return (i & ~6) | (x << 1)

    first, second = [], []
    for i in range(count):
        x = x_of(i)
        if i & 1 == 0:
            first.append((with_x(i, x ^ 1), (x & 1) ^ (x >> 1)))
            second.append((with_x(i, 3 - x), x >> 1))
        else:
            first.append((with_x(i, 3 - x), x >> 1))
            second.append((with_x(i, x ^ 1), x & 1))
    stages.append(first)
    stages.append(second)
    stages.append([(i ^ 8, (i >> 3) & 1) for i in range(count)])
    for s, stage in enumerate(stages):
        for i, (j, k) in enumerate(stage):
            assert stage[j][0] == i and stage[j][1] != k
            for t in range(s):
                assert stages[t][i][1] == stages[t][j][1]
    share = [0] * count
    for i in range(count):
        for stage in stages:
            share[i] = share[i] * 2 + stage[i][1]
    assert sorted(share) == list(range(count))
    return stages, share


def keep_bits(stages, share):
    table = np.array([[stage[i][1] for stage in stages] for i in range(len(share))], np.int32)
    idx = lax.axis_index("aux")
    bits = jnp.asarray(table)[idx]
    return [bits[s] for s in range(len(stages))], jnp.asarray(np.array(share, np.int32))[idx]


def reduce_scatter_rows(value, stages, bits):
    for stage, bit in zip(stages, bits):
        half = value.shape[0] // 2
        pairs = [(i, j) for i, (j, _) in enumerate(stage)]
        keep = lax.dynamic_slice_in_dim(value, bit * half, half, 0)
        send = lax.dynamic_slice_in_dim(value, (1 - bit) * half, half, 0)
        value = keep + lax.ppermute(send, "aux", pairs)
    return value


def all_gather_rows(value, stages, bits):
    for stage, bit in reversed(list(zip(stages, bits))):
        rows = value.shape[0]
        pairs = [(i, j) for i, (j, _) in enumerate(stage)]
        got = lax.ppermute(value, "aux", pairs)
        out = jnp.zeros((2 * rows,) + value.shape[1:], value.dtype)
        out = lax.dynamic_update_slice_in_dim(out, value, bit * rows, 0)
        value = lax.dynamic_update_slice_in_dim(out, got, (1 - bit) * rows, 0)
    return value


def body(factors, eps_occ, eps_vir):
    aux_dev, occ_dev, virt = factors.shape
    width = occ_dev * virt
    group = lax.axis_index("occ")
    groups = lax.axis_size("occ")
    aux_count = lax.axis_size("aux")
    stages, share = aux_stages(aux_count)
    bits, my_share = keep_bits(stages, share)
    rows = width // aux_count

    own = factors.reshape(aux_dev, width)
    below = passed_along(factors, "occ", 1).reshape(aux_dev, width)
    above = passed_along(factors, "occ", -1).reshape(aux_dev, width)

    own_vals = pair_values(eps_occ, eps_vir, group, occ_dev)
    up_vals = pair_values(eps_occ, eps_vir, (group + 1) % groups, occ_dev)
    my_vals = lax.dynamic_slice_in_dim(own_vals, my_share * rows, rows)
    dn_vals = pair_values(eps_occ, eps_vir, (group + groups - 1) % groups, occ_dev)
    my_dn_vals = lax.dynamic_slice_in_dim(dn_vals, my_share * rows, rows)

    contract_p = (((0,), (0,)), ((), ()))
    contract_b = (((1,), (1,)), ((), ()))
    diag = lax.dot_general(own, own, contract_p, precision=PREC,
                           preferred_element_type=jnp.float32)
    diag_share = reduce_scatter_rows(diag, stages, bits)
    diag_amp = diag_share / (my_vals[:, None] + own_vals[None, :])
    above, below, diag_amp = lax.optimization_barrier((above, below, diag_amp))
    diag_full = all_gather_rows(diag_amp, stages, bits)
    t_own = lax.dot_general(own, diag_full, contract_b, precision=PREC,
                            preferred_element_type=jnp.float32)

    up = lax.dot_general(own, above, contract_p, precision=PREC,
                         preferred_element_type=jnp.float32)
    up_share = reduce_scatter_rows(up, stages, bits)
    up_amp = up_share / (my_vals[:, None] + up_vals[None, :])
    prev_amp = passed_along(up_share, "occ", 1) / (my_dn_vals[:, None] + own_vals[None, :])
    up_full = all_gather_rows(up_amp, stages, bits)
    prev_full = all_gather_rows(prev_amp, stages, bits)
    t_up = lax.dot_general(above, up_full, contract_b, precision=PREC,
                           preferred_element_type=jnp.float32)
    t_prev = lax.dot_general(below, prev_full, (((1,), (0,)), ((), ())),
                             precision=PREC, preferred_element_type=jnp.float32)
    total = t_own + t_up + t_prev
    return (1.3 * total).reshape(aux_dev, occ_dev, virt)


def solution(mesh):
    return jax.shard_map(
        body,
        mesh=mesh,
        in_specs=(P("aux", "occ", None), P(), P()),
        out_specs=P("aux", "occ", None),
        check_vma=False,
    )
```

```python
import jax
import jax.numpy as jnp
import numpy as np
from jax import lax
from jax.sharding import PartitionSpec as P


PREC = lax.Precision.HIGH


def passed_along(value, axis, steps):
    count = lax.axis_size(axis)
    pairs = [(source, (source + steps) % count) for source in range(count)]
    return lax.ppermute(value, axis, pairs)


def pair_values(eps_occ, eps_vir, group, occ_dev):
    occ_part = lax.dynamic_slice_in_dim(eps_occ, group * occ_dev, occ_dev)
    return (occ_part[:, None] - eps_vir[None, :]).reshape(-1)


def aux_stages(count):
    assert count == 16
    stages = []
    core = [(i ^ 1, i & 1) for i in range(count)]
    stages.append(core)

    def x_of(i):
        return (i >> 1) & 3

    def with_x(i, x):
        return (i & ~6) | (x << 1)

    first, second = [], []
    for i in range(count):
        x = x_of(i)
        if i & 1 == 0:
            first.append((with_x(i, x ^ 1), (x & 1) ^ (x >> 1)))
            second.append((with_x(i, 3 - x), x >> 1))
        else:
            first.append((with_x(i, 3 - x), x >> 1))
            second.append((with_x(i, x ^ 1), x & 1))
    stages.append(first)
    stages.append(second)
    stages.append([(i ^ 8, (i >> 3) & 1) for i in range(count)])
    for s, stage in enumerate(stages):
        for i, (j, k) in enumerate(stage):
            assert stage[j][0] == i and stage[j][1] != k
            for t in range(s):
                assert stages[t][i][1] == stages[t][j][1]
    share = [0] * count
    for i in range(count):
        for stage in stages:
            share[i] = share[i] * 2 + stage[i][1]
    assert sorted(share) == list(range(count))
    return stages, share


def keep_bits(stages, share):
    table = np.array([[stage[i][1] for stage in stages] for i in range(len(share))], np.int32)
    idx = lax.axis_index("aux")
    bits = jnp.asarray(table)[idx]
    return [bits[s] for s in range(len(stages))], jnp.asarray(np.array(share, np.int32))[idx]


def reduce_scatter_rows(value, stages, bits):
    for stage, bit in zip(stages, bits):
        half = value.shape[0] // 2
        pairs = [(i, j) for i, (j, _) in enumerate(stage)]
        keep = lax.dynamic_slice_in_dim(value, bit * half, half, 0)
        send = lax.dynamic_slice_in_dim(value, (1 - bit) * half, half, 0)
        got = lax.ppermute(send, "aux", pairs)
        value = keep + got
    return value


def all_gather_rows(value, stages, bits):
    for stage, bit in reversed(list(zip(stages, bits))):
        rows = value.shape[0]
        pairs = [(i, j) for i, (j, _) in enumerate(stage)]
        got = lax.ppermute(value, "aux", pairs)
        out = jnp.zeros((2 * rows,) + value.shape[1:], value.dtype)
        out = lax.dynamic_update_slice_in_dim(out, value, bit * rows, 0)
        value = lax.dynamic_update_slice_in_dim(out, got, (1 - bit) * rows, 0)
    return value


def body(factors, eps_occ, eps_vir):
    aux_dev, occ_dev, virt = factors.shape
    width = occ_dev * virt
    group = lax.axis_index("occ")
    groups = lax.axis_size("occ")
    aux_count = lax.axis_size("aux")
    stages, share = aux_stages(aux_count)
    bits, my_share = keep_bits(stages, share)
    rows = width // aux_count

    own = factors.reshape(aux_dev, width)
    below = passed_along(factors, "occ", 1).reshape(aux_dev, width)
    above = passed_along(factors, "occ", -1).reshape(aux_dev, width)

    own_vals = pair_values(eps_occ, eps_vir, group, occ_dev)
    up_vals = pair_values(eps_occ, eps_vir, (group + 1) % groups, occ_dev)
    my_vals = lax.dynamic_slice_in_dim(own_vals, my_share * rows, rows)

    contract_p = (((0,), (0,)), ((), ()))
    contract_b = (((1,), (1,)), ((), ()))
    diag = lax.dot_general(own, own, contract_p, precision=PREC,
                           preferred_element_type=jnp.float32)
    diag_share = reduce_scatter_rows(diag, stages, bits)
    diag_amp = diag_share / (my_vals[:, None] + own_vals[None, :])
    above, below, diag_amp = lax.optimization_barrier((above, below, diag_amp))
    diag_full = all_gather_rows(diag_amp, stages, bits)
    t_own = lax.dot_general(own, diag_full, contract_b, precision=PREC,
                            preferred_element_type=jnp.float32)

    up = lax.dot_general(own, above, contract_p, precision=PREC,
                         preferred_element_type=jnp.float32)
    up_share = reduce_scatter_rows(up, stages, bits)
    up_amp = up_share / (my_vals[:, None] + up_vals[None, :])
    prev_amp = passed_along(up_amp, "occ", 1)
    up_full = all_gather_rows(up_amp, stages, bits)
    prev_full = all_gather_rows(prev_amp, stages, bits)
    t_up = lax.dot_general(above, up_full, contract_b, precision=PREC,
                           preferred_element_type=jnp.float32)
    t_prev = lax.dot_general(below, prev_full, (((1,), (0,)), ((), ())),
                             precision=PREC, preferred_element_type=jnp.float32)
    total = t_own + t_up + t_prev
    return (1.3 * total).reshape(aux_dev, occ_dev, virt)


def solution(mesh):
    return jax.shard_map(
        body,
        mesh=mesh,
        in_specs=(P("aux", "occ", None), P(), P()),
        out_specs=P("aux", "occ", None),
        check_vma=False,
    )
```
